256 devices in a mesh: dp: 2 (over core), expert: 8 (over y, x_lo), mp: 16 (over z, x_hi).
Axes of the slice: x: 4 (x_hi: 2, x_lo: 2; x = x_hi * 2 + x_lo), y: 4, z: 8, core: 2. Of those that a mesh axis runs over, the one named last changes fastest.
Arguments:
- hidden_in: bfloat16 [8192, 2048], P(('dp', 'expert')), may hold values from -6 to 6
- norm_gain: float32 [2048], replicated, may hold values from 0.1 to 1.9
- router_w: bfloat16 [2048, 8], replicated, may hold values from -0.0625 to 0.0625
- choices: int32 [8192, 2], P(('dp', 'expert')), may hold values from 0 to 7, all different within a row; in each aligned block of 512 rows (0 to 511, 512 to 1023, ...) at most 192 rows name the same one
- w_gate: bfloat16 [8, 2048, 5632], P('expert', None, 'mp'), may hold values from -0.125 to 0.125
- w_up: bfloat16 [8, 2048, 5632], P('expert', None, 'mp'), may hold values from -0.125 to 0.125
- w_down: bfloat16 [8, 5632, 2048], P('expert', 'mp'), may hold values from -0.109375 to 0.109375
Outputs:
- block_out: bfloat16 [8192, 2048], P(('dp', 'expert'), 'mp')
The draws below stay inside these ranges and needn't reach their ends.
Inputs may be any that keep to these rules, and one draw needn't show every extreme that they name: `choices`: each row names two different experts. Among the 512 rows of one block of tokens no expert is named more than 192 times, and in every draw some expert is named exactly 192 times in some block.
All inputs are finite; a program needn't handle non-finite values.
Results may differ from the reference program's by a relative error of at most 0.012.
Values may be sent and summed in bfloat16 or wider, within the bound.
No kernel may reach another device: no remote copies, remote signals or barrier semaphores. Data moves between devices by JAX's collectives and lax.ppermute only.
A program may use at most 128 MiB of HBM per device.

```python
import math
import jax
import jax.numpy as jnp
import numpy as np
from jax import lax

D = 2048
FF = 5632
TOK_DEV = 512
E = 8
CAP = 192
TOKENS = 8192
N_DP = 2
N_EXPERT = 8
N_MP = 16


def spiked(array, rng, source, target, shards_of, factor):
    def block_of(dim):
        return (jnp.arange(array.shape[dim]) // (array.shape[dim] // shards_of)).reshape((-1,) + (1,) * (array.ndim - 1 - dim))

    one_side = jax.random.permutation(rng, shards_of)[block_of(target)]
    other_side = (block_of(target) + shards_of // 2) % shards_of
    return jnp.where((block_of(source) == one_side) | (block_of(source) == other_side), factor * array, array)


def steps_of(rng, dims, shards, least, high):
    def one(axis_at, blocks):
        heights = jax.random.uniform(jax.random.fold_in(jax.random.fold_in(rng, 6), axis_at), (blocks,), jnp.float32, least / len(shards), high / len(shards))
        return jnp.repeat(jnp.exp(heights), dims[axis_at] // blocks).reshape((-1,) + (1,) * (len(dims) - axis_at - 1))

    gain = one(*shards[0])
    for cut in shards[1:]:
        gain = gain * one(*cut)
    return gain


def shared_out(rng, own, number, rows, count, top, most, lean):
    ranking = jax.random.permutation(rng, count)
    heavy_load, usual = portions_of(count, rows * top, most, lean, True), portions_of(count, rows * top, most, lean, False)
    places = jnp.arange(count)

    def named(sizes, rotation):
        used = int((sizes > 0).sum())
        fixed = max(1, used // 4)
        passed = fixed + (places - fixed + rotation * (used - fixed)) % max(1, count - fixed)
        return jnp.zeros((count,), jnp.int32).at[ranking[jnp.where(places < fixed, places, passed)]].set(jnp.asarray(sizes, jnp.int32))

    sizes = jnp.where(number % 4 == 0, named(heavy_load, number // 4), named(usual, number - number // 4 - 1))
    mixed = jax.random.permutation(jax.random.fold_in(own, 3), count)
    donor, receiver = mixed[0:count // 2 * 2:2], mixed[1:count // 2 * 2:2]
    margin = jnp.minimum(sizes[donor] - 1, most - sizes[receiver]) // 2
    margin = jnp.where((donor == ranking[0]) | (receiver == ranking[0]) | (sizes[receiver] == 0), 0, jnp.maximum(margin, 0))
    passed = jax.random.randint(jax.random.fold_in(own, 4), (count // 2,), 0, 1 << 20) % (margin + 1)
    sizes = sizes.at[donor].add(-passed).at[receiver].add(passed)
    labels = jnp.searchsorted(jnp.cumsum(sizes), jnp.arange(rows * top), side="right").astype(jnp.int32)
    grid = labels.reshape(top, rows).T
    grid = grid[jax.random.permutation(jax.random.fold_in(own, 1), rows)]
    rotation = jax.random.randint(jax.random.fold_in(own, 2), (rows, 1), 0, top)
    return jnp.take_along_axis(grid, (jnp.arange(top)[None, :] + rotation) % top, axis=1)


def portions_of(count, total, limit, skew, full):
    weights = [(1 << 20) // math.isqrt(standing ** skew) + 1 for standing in range(1, count + 1)]
    largest = limit if full else min(limit, max(-(-total // count), total * weights[0] // sum(weights)))
    least = 1 if total - largest >= count - 1 else 0
    given, rest = [largest] + [least] * (count - 1), total - largest - least * (count - 1)
    while rest > 0:
        candidates = [i for i in range(1, count) if given[i] < largest] or [i for i in range(1, count) if given[i] < limit]
        whole, budget = sum([weights[i] for i in candidates]), rest
        for i in candidates:
            addition = min(limit - given[i], max(1, budget * weights[i] // whole), rest)
            given[i] = given[i] + addition
            rest = rest - addition
    return np.array(given)


def bell_draw(rng, shape, scale, most, cuts=(), kind=jnp.bfloat16):
    loudness = steps_of(rng, shape, cuts, -0.22, 0.18) if cuts else 1.0
    entries = jax.random.normal(rng, shape, jnp.float32) * scale * loudness
    return jnp.minimum(jnp.maximum(entries, -most), most).astype(kind)


def heavy_noise(stream_key, dims, width, most, split, heavy, held_as=jnp.bfloat16):
    array = width * jax.random.normal(stream_key, dims, jnp.float32)
    if split:
        array = array * steps_of(stream_key, dims, split, -0.22, 0.18)
    return jnp.clip(spiked(array, jax.random.fold_in(stream_key, 3), *heavy), -most, most).astype(held_as)


def setup_inputs(seed: int = 0) -> dict:
    key_list = jax.random.split(jax.random.key(seed), 8)
    hidden_in = bell_draw(key_list[0], (TOKENS, D), 1.0, 6.0, ((0, 16),))
    norm_gain = jnp.clip(1.0 + 0.18 * jax.random.normal(key_list[1], (D,), jnp.float32), 0.1, 1.9)
    router_w = bell_draw(key_list[2], (D, E), (D * 4) ** -0.5, 0.0625)
    choices_keys = jax.random.split(jax.random.fold_in(key_list[3], 1), TOKENS // TOK_DEV)
    choices_turns = jax.random.permutation(jax.random.fold_in(key_list[3], 3), TOKENS // TOK_DEV)
    choices = jax.vmap(lambda own, number: shared_out(jax.random.fold_in(key_list[3], 2), own, number, TOK_DEV, E, 2, CAP, 2))(choices_keys, choices_turns).reshape((TOKENS, 2))
    w_gate = bell_draw(key_list[4], (E, D, FF), D ** -0.5, 0.125, ((0, 8), (2, 16)))
    w_up = bell_draw(key_list[5], (E, D, FF), D ** -0.5, 0.125, ((0, 8), (2, 16)))
    w_down = heavy_noise(key_list[6], (E, FF, D), FF ** -0.5, 0.109375, ((0, 8), (1, 16)), (1, 2, 16, 2.0))
    return dict(hidden_in=hidden_in, norm_gain=norm_gain, router_w=router_w, choices=choices, w_gate=w_gate, w_up=w_up, w_down=w_down)


eps_norm = 1e-06

def pair_slots(choice_ids, expert_count):
    flat_ids = choice_ids.reshape(-1).astype(jnp.int32)
    onehot = (flat_ids[:, None] == jnp.arange(expert_count, dtype=jnp.int32)[None, :]).astype(jnp.int32)
    earlier = (jnp.cumsum(onehot, axis=0) - onehot).astype(jnp.int32)
    slot_ids = lax.optimization_barrier(jnp.sum(earlier * onehot, axis=1)).astype(jnp.int32)
    return (flat_ids, slot_ids)

def pair_weights(normed, router_w, choice_ids):
    logits = jnp.dot(normed, router_w, preferred_element_type=jnp.float32)
    picked = jnp.take_along_axis(logits, choice_ids, axis=1)
    first_weight = jax.nn.sigmoid(picked[:, 0] - picked[:, 1])
    return jnp.stack([first_weight, 1.0 - first_weight], axis=1)

def reference(hidden_in, norm_gain, router_w, choices, w_gate, w_up, w_down):
    groups = N_DP * N_EXPERT
    wide_in = hidden_in.astype(jnp.float32)
    normed = (wide_in * lax.rsqrt(lax.optimization_barrier(jnp.mean(wide_in * wide_in, axis=1, keepdims=True)) + eps_norm) * norm_gain).astype(jnp.bfloat16)
    weights = pair_weights(normed, router_w, choices)
    grouped_ids = choices.reshape(groups, TOK_DEV, 2)
    flat_ids, slot_ids = jax.vmap(lambda block_ids: pair_slots(block_ids, E))(grouped_ids)
    group_ids = jnp.arange(groups, dtype=jnp.int32)[:, None]
    row_index = ((group_ids * E + flat_ids) * CAP + slot_ids).astype(jnp.int32).reshape(-1)
    sources = jnp.repeat(normed.reshape(groups, TOK_DEV, D), 2, axis=1).reshape(-1, D)
    buffer = jnp.zeros((groups * E * CAP, D), jnp.bfloat16).at[row_index].set(sources)
    per_expert = buffer.reshape(groups, E, CAP, D).transpose(1, 0, 2, 3).reshape(E, groups * CAP, D)

    def run_expert(operands):
        expert_rows, gate_w, up_w, down_w = operands
        gate_proj = jnp.dot(expert_rows, gate_w, preferred_element_type=jnp.float32)
        up_proj = jnp.dot(expert_rows, up_w, preferred_element_type=jnp.float32)
        hidden = (jax.nn.silu(gate_proj) * up_proj).astype(jnp.bfloat16)
        shares = hidden.reshape(expert_rows.shape[0], N_MP, FF // N_MP).astype(jnp.float32)
        down_parts = down_w.reshape(N_MP, FF // N_MP, D).astype(jnp.float32)
        partial_value = jnp.einsum('rsf,sfd->rsd', shares, down_parts).astype(jnp.bfloat16)
        return lax.optimization_barrier(jnp.sum(partial_value.astype(jnp.float32), axis=1))
    results = lax.map(run_expert, (per_expert, w_gate, w_up, w_down))
    returned = results.reshape(E, groups, CAP, D).transpose(1, 0, 2, 3).reshape(-1, D)
    picked = returned[row_index].reshape(TOKENS, 2, D)
    mixture = lax.optimization_barrier(jnp.sum(picked * weights[:, :, None], axis=1))
    return (wide_in + mixture).astype(jnp.bfloat16)
```

```python
import numpy as np

import jax
import jax.numpy as jnp
from jax import lax
from jax.sharding import Mesh
from jax.sharding import PartitionSpec as P

eps_norm = 1e-06


def pair_rows(choices, experts, capacity):
    flat_ids = choices.reshape(-1)
    pairs = flat_ids.shape[0]
    onehot = (flat_ids[:, None] == jnp.arange(experts, dtype=jnp.int32)[None, :]).astype(jnp.bfloat16)
    before = (
        jnp.arange(pairs, dtype=jnp.int32)[None, :] < jnp.arange(pairs, dtype=jnp.int32)[:, None]
    ).astype(jnp.bfloat16)
    earlier = jnp.dot(before, onehot, preferred_element_type=jnp.float32)
    slot_ids = jnp.sum(earlier * onehot.astype(jnp.float32), axis=1).astype(jnp.int32)
    return (flat_ids * capacity + slot_ids).reshape(-1, 2)


def pair_weights(normed, router_w, choice_ids):
    logits = jnp.dot(normed, router_w, preferred_element_type=jnp.float32)
    picked = jnp.take_along_axis(logits, choice_ids, axis=1)
    first_weight = jax.nn.sigmoid(picked[:, 0] - picked[:, 1])
    return jnp.stack([first_weight, 1.0 - first_weight], axis=1)


def make_per_device(expert_axes, mp_axes, experts, mp_count):
    def per_device(hidden_in, norm_gain, router_w, choices, w_gate, w_up, w_down):
        tokens_dev, model_width = hidden_in.shape
        capacity = 3 * tokens_dev // experts
        slice_width = model_width // mp_count
        rows_total = experts * capacity
        wide_in = hidden_in.astype(jnp.float32)
        normed = (
            wide_in
            * lax.rsqrt(jnp.mean(wide_in * wide_in, axis=1, keepdims=True) + eps_norm)
            * norm_gain
        ).astype(jnp.bfloat16)
        weights = pair_weights(normed, router_w, choices)
        rows = pair_rows(choices, experts, capacity)
        slots = jnp.arange(rows_total, dtype=jnp.int32)
        pick0 = rows[:, 0][None, :] == slots[:, None]
        pick1 = rows[:, 1][None, :] == slots[:, None]
        dispatch = (pick0 | pick1).astype(jnp.bfloat16)
        buffer = jnp.dot(dispatch, normed, preferred_element_type=jnp.float32).astype(jnp.bfloat16)
        buffer = buffer.reshape(experts, capacity, model_width)
        arrived = lax.all_to_all(buffer, expert_axes, split_axis=0, concat_axis=0, tiled=True)
        expert_rows = arrived.reshape(rows_total, model_width)
        gate_proj = jnp.dot(expert_rows, w_gate[0], preferred_element_type=jnp.float32)
        up_proj = jnp.dot(expert_rows, w_up[0], preferred_element_type=jnp.float32)
        hidden = (jax.nn.silu(gate_proj) * up_proj).astype(jnp.bfloat16)
        partial_t = lax.dot_general(
            w_down[0], hidden, (((0,), (1,)), ((), ())), preferred_element_type=jnp.float32
        ).astype(jnp.bfloat16)
        summed = partial_t
        for axis in mp_axes:
            summed = lax.psum_scatter(summed, axis, scatter_dimension=0, tiled=True)
        summed = summed.reshape(slice_width, experts, capacity)
        returned = lax.all_to_all(summed, expert_axes, split_axis=1, concat_axis=1, tiled=True)
        returned = returned.reshape(slice_width, rows_total)
        column = lax.axis_index(mp_axes) * slice_width
        residual = lax.dynamic_slice_in_dim(wide_in, column, slice_width, 1)
        sel0 = (rows[:, 0][:, None] == slots[None, :]).astype(jnp.bfloat16)
        sel1 = (rows[:, 1][:, None] == slots[None, :]).astype(jnp.bfloat16)
        dims = (((1,), (1,)), ((), ()))
        out0 = lax.dot_general(sel0, returned, dims, preferred_element_type=jnp.float32)
        out1 = lax.dot_general(sel1, returned, dims, preferred_element_type=jnp.float32)
        mixture = out0 * weights[:, 0:1] + out1 * weights[:, 1:2]
        return (residual + mixture).astype(jnp.bfloat16)

    return per_device


def x_parts(devices):
    coords = [getattr(d, "coords", None) for d in devices]
    if any(c is None for c in coords):
        return 1
    return len({c[0] for c in coords})


def solution(mesh):
    n_dp, n_expert, n_mp = (mesh.shape[a] for a in ("dp", "expert", "mp"))
    devs = np.asarray(mesh.devices).reshape(n_dp, n_expert, n_mp)
    ex = x_parts(devs[0, :, 0])
    mx = x_parts(devs[0, 0, :])
    if n_expert % ex or n_mp % mx:
        ex, mx = 1, 1
    fine = Mesh(
        devs.reshape(n_dp, n_expert // ex, ex, n_mp // mx, mx), ("dp", "ey", "ex", "mz", "mx")
    )
    expert_axes = ("ey", "ex")
    mp_axes = ("mz", "mx")
    tok = ("dp",) + expert_axes
    placed = (
        P(tok, None),
        P(),
        P(),
        P(tok, None),
        P(expert_axes, None, mp_axes),
        P(expert_axes, None, mp_axes),
        P(expert_axes, mp_axes, None),
    )
    return jax.shard_map(
        make_per_device(expert_axes, mp_axes, n_expert, n_mp),
        mesh=fine,
        in_specs=placed,
        out_specs=P(tok, mp_axes),
        check_vma=False,
    )
```

```python
import numpy as np

import jax
import jax.numpy as jnp
from jax import lax
from jax.sharding import Mesh
from jax.sharding import PartitionSpec as P

eps_norm = 1e-06


def pair_rows(choices, experts, capacity):
    flat_ids = choices.reshape(-1)
    pairs = flat_ids.shape[0]
    onehot = (flat_ids[:, None] == jnp.arange(experts, dtype=jnp.int32)[None, :]).astype(jnp.bfloat16)
    before = (
        jnp.arange(pairs, dtype=jnp.int32)[None, :] < jnp.arange(pairs, dtype=jnp.int32)[:, None]
    ).astype(jnp.bfloat16)
    earlier = jnp.dot(before, onehot, preferred_element_type=jnp.float32)
    slot_ids = jnp.sum(earlier * onehot.astype(jnp.float32), axis=1).astype(jnp.int32)
    return (flat_ids * capacity + slot_ids).reshape(-1, 2)


def pair_weights(normed, router_w, choice_ids):
    logits = jnp.dot(normed, router_w, preferred_element_type=jnp.float32)
    picked = jnp.take_along_axis(logits, choice_ids, axis=1)
    first_weight = jax.nn.sigmoid(picked[:, 0] - picked[:, 1])
    return jnp.stack([first_weight, 1.0 - first_weight], axis=1)


def make_per_device(expert_axes, mp_axes, experts, mp_count, n_chunks=2):
    def per_device(hidden_in, norm_gain, router_w, choices, w_gate, w_up, w_down):
        tokens_dev, model_width = hidden_in.shape
        capacity = 3 * tokens_dev // experts
        slice_width = model_width // mp_count
        rows_total = experts * capacity
        wide_in = hidden_in.astype(jnp.float32)
        normed = (
            wide_in
            * lax.rsqrt(jnp.mean(wide_in * wide_in, axis=1, keepdims=True) + eps_norm)
            * norm_gain
        ).astype(jnp.bfloat16)
        weights = pair_weights(normed, router_w, choices)
        rows = pair_rows(choices, experts, capacity)
        slots = jnp.arange(rows_total, dtype=jnp.int32)
        pick0 = rows[:, 0][None, :] == slots[:, None]
        pick1 = rows[:, 1][None, :] == slots[:, None]
        dispatch = (pick0 | pick1).astype(jnp.bfloat16)
        buffer = jnp.dot(dispatch, normed, preferred_element_type=jnp.float32).astype(jnp.bfloat16)
        buffer = buffer.reshape(experts, capacity, model_width)
        chunk = capacity // n_chunks
        pieces = []
        for c in range(n_chunks):
            part = buffer[:, c * chunk:(c + 1) * chunk]
            arrived = lax.all_to_all(part, expert_axes, split_axis=0, concat_axis=0, tiled=True)
            expert_rows = arrived.reshape(experts * chunk, model_width)
            gate_proj = jnp.dot(expert_rows, w_gate[0], preferred_element_type=jnp.float32)
            up_proj = jnp.dot(expert_rows, w_up[0], preferred_element_type=jnp.float32)
            hidden = (jax.nn.silu(gate_proj) * up_proj).astype(jnp.bfloat16)
            partial_t = lax.dot_general(
                w_down[0], hidden, (((0,), (1,)), ((), ())), preferred_element_type=jnp.float32
            ).astype(jnp.bfloat16)
            summed = partial_t
            for axis in mp_axes:
                summed = lax.psum_scatter(summed, axis, scatter_dimension=0, tiled=True)
            summed = summed.reshape(slice_width, experts, chunk)
            pieces.append(
                lax.all_to_all(summed, expert_axes, split_axis=1, concat_axis=1, tiled=True)
            )
        returned = jnp.concatenate(pieces, axis=2).reshape(slice_width, rows_total)
        column = lax.axis_index(mp_axes) * slice_width
        residual = lax.dynamic_slice_in_dim(wide_in, column, slice_width, 1)
        sel0 = (rows[:, 0][:, None] == slots[None, :]).astype(jnp.bfloat16)
        sel1 = (rows[:, 1][:, None] == slots[None, :]).astype(jnp.bfloat16)
        dims = (((1,), (1,)), ((), ()))
        out0 = lax.dot_general(sel0, returned, dims, preferred_element_type=jnp.float32)
        out1 = lax.dot_general(sel1, returned, dims, preferred_element_type=jnp.float32)
        mixture = out0 * weights[:, 0:1] + out1 * weights[:, 1:2]
        return (residual + mixture).astype(jnp.bfloat16)

    return per_device


def x_parts(devices):
    coords = [getattr(d, "coords", None) for d in devices]
    if any(c is None for c in coords):
        return 1
    return len({c[0] for c in coords})


def solution(mesh):
    n_dp, n_expert, n_mp = (mesh.shape[a] for a in ("dp", "expert", "mp"))
    devs = np.asarray(mesh.devices).reshape(n_dp, n_expert, n_mp)
    ex = x_parts(devs[0, :, 0])
    mx = x_parts(devs[0, 0, :])
    if n_expert % ex or n_mp % mx:
        ex, mx = 1, 1
    fine = Mesh(
        devs.reshape(n_dp, n_expert // ex, ex, n_mp // mx, mx), ("dp", "ey", "ex", "mz", "mx")
    )
    expert_axes = ("ey", "ex")
    mp_axes = ("mz", "mx")
    tok = ("dp",) + expert_axes
    placed = (
        P(tok, None),
        P(),
        P(),
        P(tok, None),
        P(expert_axes, None, mp_axes),
        P(expert_axes, None, mp_axes),
        P(expert_axes, mp_axes, None),
    )
    return jax.shard_map(
        make_per_device(expert_axes, mp_axes, n_expert, n_mp),
        mesh=fine,
        in_specs=placed,
        out_specs=P(tok, mp_axes),
        check_vma=False,
    )
```

```python
import numpy as np

import jax
import jax.numpy as jnp
from jax import lax
from jax.sharding import Mesh
from jax.sharding import PartitionSpec as P

eps_norm = 1e-06


def pair_rows(choices, experts, capacity):
    flat_ids = choices.reshape(-1)
    pairs = flat_ids.shape[0]
    onehot = (flat_ids[:, None] == jnp.arange(experts, dtype=jnp.int32)[None, :]).astype(jnp.bfloat16)
    before = (
        jnp.arange(pairs, dtype=jnp.int32)[None, :] < jnp.arange(pairs, dtype=jnp.int32)[:, None]
    ).astype(jnp.bfloat16)
    earlier = jnp.dot(before, onehot, preferred_element_type=jnp.float32)
    slot_ids = jnp.sum(earlier * onehot.astype(jnp.float32), axis=1).astype(jnp.int32)
    return (flat_ids * capacity + slot_ids).reshape(-1, 2)


def pair_weights(normed, router_w, choice_ids):
    logits = jnp.dot(normed, router_w, preferred_element_type=jnp.float32)
    picked = jnp.take_along_axis(logits, choice_ids, axis=1)
    first_weight = jax.nn.sigmoid(picked[:, 0] - picked[:, 1])
    return jnp.stack([first_weight, 1.0 - first_weight], axis=1)


def pair_exchange(summed, axis):
    n = lax.axis_size(axis)
    if n == 1:
        return summed
    own = lax.axis_index(axis)
    width = summed.shape[0] // 2
    keep = lax.dynamic_slice_in_dim(summed, own * width, width, 0)
    give = lax.dynamic_slice_in_dim(summed, (1 - own) * width, width, 0)
    got = lax.ppermute(give, axis, [(0, 1), (1, 0)])
    return (keep.astype(jnp.float32) + got.astype(jnp.float32)).astype(jnp.bfloat16)


def make_per_device(expert_axes, mp_axes, experts, mp_count, n_chunks=2):
    def per_device(hidden_in, norm_gain, router_w, choices, w_gate, w_up, w_down):
        tokens_dev, model_width = hidden_in.shape
        capacity = 3 * tokens_dev // experts
        slice_width = model_width // mp_count
        rows_total = experts * capacity
        wide_in = hidden_in.astype(jnp.float32)
        normed = (
            wide_in
            * lax.rsqrt(jnp.mean(wide_in * wide_in, axis=1, keepdims=True) + eps_norm)
            * norm_gain
        ).astype(jnp.bfloat16)
        weights = pair_weights(normed, router_w, choices)
        rows = pair_rows(choices, experts, capacity)
        slots = jnp.arange(rows_total, dtype=jnp.int32)
        pick0 = rows[:, 0][None, :] == slots[:, None]
        pick1 = rows[:, 1][None, :] == slots[:, None]
        dispatch = (pick0 | pick1).astype(jnp.bfloat16)
        buffer = jnp.dot(dispatch, normed, preferred_element_type=jnp.float32).astype(jnp.bfloat16)
        buffer = buffer.reshape(experts, capacity, model_width)
        chunk = capacity // n_chunks
        pieces = []
        for c in range(n_chunks):
            part = buffer[:, c * chunk:(c + 1) * chunk]
            arrived = lax.all_to_all(part, expert_axes, split_axis=0, concat_axis=0, tiled=True)
            expert_rows = arrived.reshape(experts * chunk, model_width)
            gate_proj = jnp.dot(expert_rows, w_gate[0], preferred_element_type=jnp.float32)
            up_proj = jnp.dot(expert_rows, w_up[0], preferred_element_type=jnp.float32)
            hidden = (jax.nn.silu(gate_proj) * up_proj).astype(jnp.bfloat16)
            partial_t = lax.dot_general(
                w_down[0], hidden, (((0,), (1,)), ((), ())), preferred_element_type=jnp.float32
            ).astype(jnp.bfloat16)
            summed = lax.psum_scatter(partial_t, mp_axes[0], scatter_dimension=0, tiled=True)
            summed = pair_exchange(summed, mp_axes[1])
            summed = summed.reshape(slice_width, experts, chunk)
            pieces.append(
                lax.all_to_all(summed, expert_axes, split_axis=1, concat_axis=1, tiled=True)
            )
        returned = jnp.concatenate(pieces, axis=2).reshape(slice_width, rows_total)
        column = lax.axis_index(mp_axes) * slice_width
        residual = lax.dynamic_slice_in_dim(wide_in, column, slice_width, 1)
        sel0 = (rows[:, 0][:, None] == slots[None, :]).astype(jnp.bfloat16)
        sel1 = (rows[:, 1][:, None] == slots[None, :]).astype(jnp.bfloat16)
        dims = (((1,), (1,)), ((), ()))
        out0 = lax.dot_general(sel0, returned, dims, preferred_element_type=jnp.float32)
        out1 = lax.dot_general(sel1, returned, dims, preferred_element_type=jnp.float32)
        mixture = out0 * weights[:, 0:1] + out1 * weights[:, 1:2]
        return (residual + mixture).astype(jnp.bfloat16)

    return per_device


def x_parts(devices):
    coords = [getattr(d, "coords", None) for d in devices]
    if any(c is None for c in coords):
        return 1
    return len({c[0] for c in coords})


def solution(mesh):
    n_dp, n_expert, n_mp = (mesh.shape[a] for a in ("dp", "expert", "mp"))
    devs = np.asarray(mesh.devices).reshape(n_dp, n_expert, n_mp)
    ex = x_parts(devs[0, :, 0])
    mx = x_parts(devs[0, 0, :])
    if n_expert % ex or n_mp % mx:
        ex, mx = 1, 1
    fine = Mesh(
        devs.reshape(n_dp, n_expert // ex, ex, n_mp // mx, mx), ("dp", "ey", "ex", "mz", "mx")
    )
    expert_axes = ("ey", "ex")
    mp_axes = ("mz", "mx")
    tok = ("dp",) + expert_axes
    placed = (
        P(tok, None),
        P(),
        P(),
        P(tok, None),
        P(expert_axes, None, mp_axes),
        P(expert_axes, None, mp_axes),
        P(expert_axes, mp_axes, None),
    )
    return jax.shard_map(
        make_per_device(expert_axes, mp_axes, n_expert, n_mp),
        mesh=fine,
        in_specs=placed,
        out_specs=P(tok, mp_axes),
        check_vma=False,
    )
```

```python
import numpy as np

import jax
import jax.numpy as jnp
from jax import lax
from jax.sharding import Mesh
from jax.sharding import PartitionSpec as P

eps_norm = 1e-06


def pair_slots(choices, experts):
    tokens = choices.shape[0]
    ids = jnp.arange(experts, dtype=jnp.int32)[None, :]
    oh0 = (choices[:, 0:1] == ids).astype(jnp.float32)
    oh1 = (choices[:, 1:2] == ids).astype(jnp.float32)
    tri = (
        jnp.arange(tokens, dtype=jnp.int32)[None, :] < jnp.arange(tokens, dtype=jnp.int32)[:, None]
    ).astype(jnp.bfloat16)
    cnt = jnp.dot(tri, (oh0 + oh1).astype(jnp.bfloat16), preferred_element_type=jnp.float32)
    slot0 = jnp.sum(cnt * oh0, axis=1)
    slot1 = jnp.sum((cnt + oh0) * oh1, axis=1)
    return slot0.astype(jnp.int32), slot1.astype(jnp.int32), oh0, oh1


def pair_weights(logits, oh0, oh1):
    picked0 = jnp.sum(logits * oh0, axis=1)
    picked1 = jnp.sum(logits * oh1, axis=1)
    first_weight = jax.nn.sigmoid(picked0 - picked1)
    return first_weight, 1.0 - first_weight


def pair_exchange(summed, axis):
    n = lax.axis_size(axis)
    if n == 1:
        return summed
    own = lax.axis_index(axis)
    width = summed.shape[0] // 2
    keep = lax.dynamic_slice_in_dim(summed, own * width, width, 0)
    give = lax.dynamic_slice_in_dim(summed, (1 - own) * width, width, 0)
    got = lax.ppermute(give, axis, [(0, 1), (1, 0)])
    return (keep.astype(jnp.float32) + got.astype(jnp.float32)).astype(jnp.bfloat16)


def make_per_device(expert_axes, mp_axes, experts, mp_count, n_chunks=2):
    def per_device(hidden_in, norm_gain, router_w, choices, w_gate, w_up, w_down):
        tokens_dev, model_width = hidden_in.shape
        capacity = 3 * tokens_dev // experts
        slice_width = model_width // mp_count
        rows_total = experts * capacity
        wide_in = hidden_in.astype(jnp.float32)
        normed = (
            wide_in
            * lax.rsqrt(jnp.mean(wide_in * wide_in, axis=1, keepdims=True) + eps_norm)
            * norm_gain
        ).astype(jnp.bfloat16)
        slot0, slot1, oh0, oh1 = pair_slots(choices, experts)
        chunk = capacity // n_chunks
        e0, e1 = choices[:, 0], choices[:, 1]
        chunk_rows = jnp.arange(experts * chunk, dtype=jnp.int32)
        column = lax.axis_index(mp_axes) * slice_width
        residual = lax.dynamic_slice_in_dim(wide_in, column, slice_width, 1)
        mixture = None
        results = []
        for c in range(n_chunks):
            r0 = jnp.where(slot0 // chunk == c, e0 * chunk + slot0 % chunk, -1)
            r1 = jnp.where(slot1 // chunk == c, e1 * chunk + slot1 % chunk, -1)
            dispatch = (
                (r0[None, :] == chunk_rows[:, None]) | (r1[None, :] == chunk_rows[:, None])
            ).astype(jnp.bfloat16)
            part = jnp.dot(dispatch, normed, preferred_element_type=jnp.float32).astype(jnp.bfloat16)
            part = part.reshape(experts, chunk, model_width)
            arrived = lax.all_to_all(part, expert_axes, split_axis=0, concat_axis=0, tiled=True)
            expert_rows = arrived.reshape(experts * chunk, model_width)
            gate_proj = jnp.dot(expert_rows, w_gate[0], preferred_element_type=jnp.float32)
            up_proj = jnp.dot(expert_rows, w_up[0], preferred_element_type=jnp.float32)
            hidden = (jax.nn.silu(gate_proj) * up_proj).astype(jnp.bfloat16)
            partial_t = lax.dot_general(
                w_down[0], hidden, (((0,), (1,)), ((), ())), preferred_element_type=jnp.float32
            ).astype(jnp.bfloat16)
            summed = lax.psum_scatter(partial_t, mp_axes[0], scatter_dimension=0, tiled=True)
            summed = pair_exchange(summed, mp_axes[1])
            summed = summed.reshape(slice_width, experts, chunk)
            returned = lax.all_to_all(summed, expert_axes, split_axis=1, concat_axis=1, tiled=True)
            returned = returned.reshape(slice_width, experts * chunk)
            results.append((r0, r1, returned))
        logits = jnp.dot(normed, router_w, preferred_element_type=jnp.float32)
        w0, w1 = pair_weights(logits, oh0, oh1)
        dims = (((1,), (1,)), ((), ()))
        for r0, r1, returned in results:
            sel0 = (r0[:, None] == chunk_rows[None, :]).astype(jnp.bfloat16)
            sel1 = (r1[:, None] == chunk_rows[None, :]).astype(jnp.bfloat16)
            out0 = lax.dot_general(sel0, returned, dims, preferred_element_type=jnp.float32)
            out1 = lax.dot_general(sel1, returned, dims, preferred_element_type=jnp.float32)
            term = out0 * w0[:, None] + out1 * w1[:, None]
            mixture = term if mixture is None else mixture + term
        return (residual + mixture).astype(jnp.bfloat16)

    return per_device


def x_parts(devices):
    coords = [getattr(d, "coords", None) for d in devices]
    if any(c is None for c in coords):
        return 1
    return len({c[0] for c in coords})


def solution(mesh):
    n_dp, n_expert, n_mp = (mesh.shape[a] for a in ("dp", "expert", "mp"))
    devs = np.asarray(mesh.devices).reshape(n_dp, n_expert, n_mp)
    ex = x_parts(devs[0, :, 0])
    mx = x_parts(devs[0, 0, :])
    if n_expert % ex or n_mp % mx:
        ex, mx = 1, 1
    fine = Mesh(
        devs.reshape(n_dp, n_expert // ex, ex, n_mp // mx, mx), ("dp", "ey", "ex", "mz", "mx")
    )
    expert_axes = ("ey", "ex")
    mp_axes = ("mz", "mx")
    tok = ("dp",) + expert_axes
    placed = (
        P(tok, None),
        P(),
        P(),
        P(tok, None),
        P(expert_axes, None, mp_axes),
        P(expert_axes, None, mp_axes),
        P(expert_axes, mp_axes, None),
    )
    return jax.shard_map(
        make_per_device(expert_axes, mp_axes, n_expert, n_mp),
        mesh=fine,
        in_specs=placed,
        out_specs=P(tok, mp_axes),
        check_vma=False,
    )
```

```python
import numpy as np

import jax
import jax.numpy as jnp
from jax import lax
from jax.sharding import Mesh
from jax.sharding import PartitionSpec as P

eps_norm = 1e-06


def pair_slots(choices, experts):
    tokens = choices.shape[0]
    ids = jnp.arange(experts, dtype=jnp.int32)[None, :]
    oh0 = (choices[:, 0:1] == ids).astype(jnp.float32)
    oh1 = (choices[:, 1:2] == ids).astype(jnp.float32)
    tri = (
        jnp.arange(tokens, dtype=jnp.int32)[None, :] < jnp.arange(tokens, dtype=jnp.int32)[:, None]
    ).astype(jnp.bfloat16)
    cnt = jnp.dot(tri, (oh0 + oh1).astype(jnp.bfloat16), preferred_element_type=jnp.float32)
    slot0 = jnp.sum(cnt * oh0, axis=1)
    slot1 = jnp.sum((cnt + oh0) * oh1, axis=1)
    return slot0.astype(jnp.int32), slot1.astype(jnp.int32), oh0, oh1


def pair_weights(logits, oh0, oh1):
    picked0 = jnp.sum(logits * oh0, axis=1)
    picked1 = jnp.sum(logits * oh1, axis=1)
    first_weight = jax.nn.sigmoid(picked0 - picked1)
    return first_weight, 1.0 - first_weight


def pair_exchange(summed, axis):
    n = lax.axis_size(axis)
    if n == 1:
        return summed
    own = lax.axis_index(axis)
    width = summed.shape[0] // 2
    keep = lax.dynamic_slice_in_dim(summed, own * width, width, 0)
    give = lax.dynamic_slice_in_dim(summed, (1 - own) * width, width, 0)
    got = lax.ppermute(give, axis, [(0, 1), (1, 0)])
    return (keep.astype(jnp.float32) + got.astype(jnp.float32)).astype(jnp.bfloat16)


def make_per_device(expert_axes, mp_axes, experts, mp_count, n_chunks=2):
    def per_device(hidden_in, norm_gain, router_w, choices, w_gate, w_up, w_down):
        tokens_dev, model_width = hidden_in.shape
        capacity = 3 * tokens_dev // experts
        slice_width = model_width // mp_count
        rows_total = experts * capacity
        wide_in = hidden_in.astype(jnp.float32)
        normed = (
            wide_in
            * lax.rsqrt(jnp.mean(wide_in * wide_in, axis=1, keepdims=True) + eps_norm)
            * norm_gain
        ).astype(jnp.bfloat16)
        slot0, slot1, oh0, oh1 = pair_slots(choices, experts)
        chunk = capacity // n_chunks
        e0, e1 = choices[:, 0], choices[:, 1]
        chunk_rows = jnp.arange(experts * chunk, dtype=jnp.int32)
        column = lax.axis_index(mp_axes) * slice_width
        residual = lax.dynamic_slice_in_dim(wide_in, column, slice_width, 1)
        mixture = None
        results = []
        for c in range(n_chunks):
            r0 = jnp.where(slot0 // chunk == c, e0 * chunk + slot0 % chunk, -1)
            r1 = jnp.where(slot1 // chunk == c, e1 * chunk + slot1 % chunk, -1)
            dispatch = (
                (r0[None, :] == chunk_rows[:, None]) | (r1[None, :] == chunk_rows[:, None])
            ).astype(jnp.bfloat16)
            part = jnp.dot(dispatch, normed, preferred_element_type=jnp.float32).astype(jnp.bfloat16)
            part = part.reshape(experts, chunk, model_width)
            arrived = lax.all_to_all(part, expert_axes, split_axis=0, concat_axis=0, tiled=True)
            expert_rows = arrived.reshape(experts * chunk, model_width)
            gate_proj = jnp.dot(expert_rows, w_gate[0], preferred_element_type=jnp.float32)
            up_proj = jnp.dot(expert_rows, w_up[0], preferred_element_type=jnp.float32)
            hidden = (jax.nn.silu(gate_proj) * up_proj).astype(jnp.bfloat16)
            partial_t = lax.dot_general(
                w_down[0], hidden, (((0,), (1,)), ((), ())), preferred_element_type=jnp.float32
            ).astype(jnp.bfloat16)
            summed = lax.psum_scatter(partial_t, mp_axes[0], scatter_dimension=0, tiled=True)
            halves = lax.axis_size(mp_axes[1])
            blocks = summed.reshape(halves, slice_width, experts, chunk).transpose(2, 0, 1, 3)
            blocks = blocks.reshape(experts * halves, slice_width, chunk)
            got = lax.all_to_all(blocks, expert_axes + mp_axes[1:], split_axis=0, concat_axis=0, tiled=True)
            got = got.reshape(experts, halves, slice_width, chunk).astype(jnp.float32).sum(axis=1)
            returned = got.astype(jnp.bfloat16).transpose(1, 0, 2).reshape(slice_width, experts * chunk)
            results.append((r0, r1, returned))
        logits = jnp.dot(normed, router_w, preferred_element_type=jnp.float32)
        w0, w1 = pair_weights(logits, oh0, oh1)
        dims = (((1,), (1,)), ((), ()))
        for r0, r1, returned in results:
            sel0 = (r0[:, None] == chunk_rows[None, :]).astype(jnp.bfloat16)
            sel1 = (r1[:, None] == chunk_rows[None, :]).astype(jnp.bfloat16)
            out0 = lax.dot_general(sel0, returned, dims, preferred_element_type=jnp.float32)
            out1 = lax.dot_general(sel1, returned, dims, preferred_element_type=jnp.float32)
            term = out0 * w0[:, None] + out1 * w1[:, None]
            mixture = term if mixture is None else mixture + term
        return (residual + mixture).astype(jnp.bfloat16)

    return per_device


def x_parts(devices):
    coords = [getattr(d, "coords", None) for d in devices]
    if any(c is None for c in coords):
        return 1
    return len({c[0] for c in coords})


def solution(mesh):
    n_dp, n_expert, n_mp = (mesh.shape[a] for a in ("dp", "expert", "mp"))
    devs = np.asarray(mesh.devices).reshape(n_dp, n_expert, n_mp)
    ex = x_parts(devs[0, :, 0])
    mx = x_parts(devs[0, 0, :])
    if n_expert % ex or n_mp % mx:
        ex, mx = 1, 1
    fine = Mesh(
        devs.reshape(n_dp, n_expert // ex, ex, n_mp // mx, mx), ("dp", "ey", "ex", "mz", "mx")
    )
    expert_axes = ("ey", "ex")
    mp_axes = ("mz", "mx")
    tok = ("dp",) + expert_axes
    placed = (
        P(tok, None),
        P(),
        P(),
        P(tok, None),
        P(expert_axes, None, mp_axes),
        P(expert_axes, None, mp_axes),
        P(expert_axes, mp_axes, None),
    )
    return jax.shard_map(
        make_per_device(expert_axes, mp_axes, n_expert, n_mp),
        mesh=fine,
        in_specs=placed,
        out_specs=P(tok, mp_axes),
        check_vma=False,
    )
```

```python
import numpy as np

import jax
import jax.numpy as jnp
from jax import lax
from jax.sharding import Mesh
from jax.sharding import PartitionSpec as P

eps_norm = 1e-06


def pair_slots(choices, experts):
    tokens = choices.shape[0]
    ids = jnp.arange(experts, dtype=jnp.int32)[None, :]
    oh0 = (choices[:, 0:1] == ids).astype(jnp.float32)
    oh1 = (choices[:, 1:2] == ids).astype(jnp.float32)
    tri = (
        jnp.arange(tokens, dtype=jnp.int32)[None, :] < jnp.arange(tokens, dtype=jnp.int32)[:, None]
    ).astype(jnp.bfloat16)
    cnt = jnp.dot(tri, (oh0 + oh1).astype(jnp.bfloat16), preferred_element_type=jnp.float32)
    slot0 = jnp.sum(cnt * oh0, axis=1)
    slot1 = jnp.sum((cnt + oh0) * oh1, axis=1)
    return slot0.astype(jnp.int32), slot1.astype(jnp.int32), oh0, oh1


def pair_weights(logits, oh0, oh1):
    picked0 = jnp.sum(logits * oh0, axis=1)
    picked1 = jnp.sum(logits * oh1, axis=1)
    first_weight = jax.nn.sigmoid(picked0 - picked1)
    return first_weight, 1.0 - first_weight


def pair_exchange(summed, axis):
    n = lax.axis_size(axis)
    if n == 1:
        return summed
    own = lax.axis_index(axis)
    width = summed.shape[0] // 2
    keep = lax.dynamic_slice_in_dim(summed, own * width, width, 0)
    give = lax.dynamic_slice_in_dim(summed, (1 - own) * width, width, 0)
    got = lax.ppermute(give, axis, [(0, 1), (1, 0)])
    return (keep.astype(jnp.float32) + got.astype(jnp.float32)).astype(jnp.bfloat16)


def make_per_device(expert_axes, mp_axes, experts, mp_count, n_chunks=2):
    def per_device(hidden_in, norm_gain, router_w, choices, w_gate, w_up, w_down):
        tokens_dev, model_width = hidden_in.shape
        capacity = 3 * tokens_dev // experts
        slice_width = model_width // mp_count
        rows_total = experts * capacity
        wide_in = hidden_in.astype(jnp.float32)
        normed = (
            wide_in
            * lax.rsqrt(jnp.mean(wide_in * wide_in, axis=1, keepdims=True) + eps_norm)
            * norm_gain
        ).astype(jnp.bfloat16)
        slot0, slot1, oh0, oh1 = pair_slots(choices, experts)
        chunk = capacity // n_chunks
        e0, e1 = choices[:, 0], choices[:, 1]
        chunk_rows = jnp.arange(experts * chunk, dtype=jnp.int32)
        column = lax.axis_index(mp_axes) * slice_width
        residual = lax.dynamic_slice_in_dim(hidden_in, column, slice_width, 1).astype(jnp.float32)
        mixture = None
        ff_share = w_gate.shape[2]
        gate_up = jnp.concatenate([w_gate[0], w_up[0]], axis=1)
        results = []
        for c in range(n_chunks):
            r0 = jnp.where(slot0 // chunk == c, e0 * chunk + slot0 % chunk, -1)
            r1 = jnp.where(slot1 // chunk == c, e1 * chunk + slot1 % chunk, -1)
            dispatch = (
                (r0[None, :] == chunk_rows[:, None]) | (r1[None, :] == chunk_rows[:, None])
            ).astype(jnp.bfloat16)
            part = jnp.dot(dispatch, normed, preferred_element_type=jnp.float32).astype(jnp.bfloat16)
            part = part.reshape(experts, chunk, model_width)
            arrived = lax.all_to_all(part, expert_axes, split_axis=0, concat_axis=0, tiled=True)
            expert_rows = arrived.reshape(experts * chunk, model_width)
            both = jnp.dot(expert_rows, gate_up, preferred_element_type=jnp.float32)
            gate_proj, up_proj = both[:, :ff_share], both[:, ff_share:]
            hidden = (jax.nn.silu(gate_proj) * up_proj).astype(jnp.bfloat16)
            partial_t = lax.dot_general(
                w_down[0], hidden, (((0,), (1,)), ((), ())), preferred_element_type=jnp.float32
            ).astype(jnp.bfloat16)
            summed = lax.psum_scatter(partial_t, mp_axes[0], scatter_dimension=0, tiled=True)
            halves = lax.axis_size(mp_axes[1])
            blocks = summed.reshape(halves, slice_width, experts, chunk).transpose(2, 0, 1, 3)
            blocks = blocks.reshape(experts * halves, slice_width, chunk)
            got = lax.all_to_all(blocks, expert_axes + mp_axes[1:], split_axis=0, concat_axis=0, tiled=True)
            got = got.reshape(experts, halves, slice_width, chunk).astype(jnp.float32).sum(axis=1)
            returned = got.astype(jnp.bfloat16).transpose(1, 0, 2).reshape(slice_width, experts * chunk)
            results.append((r0, r1, returned))
        logits = jnp.dot(normed, router_w, preferred_element_type=jnp.float32)
        w0, w1 = pair_weights(logits, oh0, oh1)
        dims = (((1,), (1,)), ((), ()))
        for r0, r1, returned in results:
            sel0 = (r0[:, None] == chunk_rows[None, :]).astype(jnp.bfloat16)
            sel1 = (r1[:, None] == chunk_rows[None, :]).astype(jnp.bfloat16)
            out0 = lax.dot_general(sel0, returned, dims, preferred_element_type=jnp.float32)
            out1 = lax.dot_general(sel1, returned, dims, preferred_element_type=jnp.float32)
            term = out0 * w0[:, None] + out1 * w1[:, None]
            mixture = term if mixture is None else mixture + term
        return (residual + mixture).astype(jnp.bfloat16)

    return per_device


def x_parts(devices):
    coords = [getattr(d, "coords", None) for d in devices]
    if any(c is None for c in coords):
        return 1
    return len({c[0] for c in coords})


def solution(mesh):
    n_dp, n_expert, n_mp = (mesh.shape[a] for a in ("dp", "expert", "mp"))
    devs = np.asarray(mesh.devices).reshape(n_dp, n_expert, n_mp)
    ex = x_parts(devs[0, :, 0])
    mx = x_parts(devs[0, 0, :])
    if n_expert % ex or n_mp % mx:
        ex, mx = 1, 1
    fine = Mesh(
        devs.reshape(n_dp, n_expert // ex, ex, n_mp // mx, mx), ("dp", "ey", "ex", "mz", "mx")
    )
    expert_axes = ("ey", "ex")
    mp_axes = ("mz", "mx")
    tok = ("dp",) + expert_axes
    placed = (
        P(tok, None),
        P(),
        P(),
        P(tok, None),
        P(expert_axes, None, mp_axes),
        P(expert_axes, None, mp_axes),
        P(expert_axes, mp_axes, None),
    )
    return jax.shard_map(
        make_per_device(expert_axes, mp_axes, n_expert, n_mp),
        mesh=fine,
        in_specs=placed,
        out_specs=P(tok, mp_axes),
        check_vma=False,
    )
```

```python
import numpy as np

import jax
import jax.numpy as jnp
from jax import lax
from jax.sharding import Mesh
from jax.sharding import PartitionSpec as P

eps_norm = 1e-06


def pair_slots(choices, experts):
    tokens = choices.shape[0]
    ids = jnp.arange(experts, dtype=jnp.int32)[None, :]
    oh0 = (choices[:, 0:1] == ids).astype(jnp.float32)
    oh1 = (choices[:, 1:2] == ids).astype(jnp.float32)
    tri = (
        jnp.arange(tokens, dtype=jnp.int32)[None, :] < jnp.arange(tokens, dtype=jnp.int32)[:, None]
    ).astype(jnp.bfloat16)
    cnt = jnp.dot(tri, (oh0 + oh1).astype(jnp.bfloat16), preferred_element_type=jnp.float32)
    slot0 = jnp.sum(cnt * oh0, axis=1)
    slot1 = jnp.sum((cnt + oh0) * oh1, axis=1)
    return slot0.astype(jnp.int32), slot1.astype(jnp.int32), oh0, oh1


def pair_weights(logits, oh0, oh1):
    picked0 = jnp.sum(logits * oh0, axis=1)
    picked1 = jnp.sum(logits * oh1, axis=1)
    first_weight = jax.nn.sigmoid(picked0 - picked1)
    return first_weight, 1.0 - first_weight


def pair_exchange(summed, axis):
    n = lax.axis_size(axis)
    if n == 1:
        return summed
    own = lax.axis_index(axis)
    width = summed.shape[0] // 2
    keep = lax.dynamic_slice_in_dim(summed, own * width, width, 0)
    give = lax.dynamic_slice_in_dim(summed, (1 - own) * width, width, 0)
    got = lax.ppermute(give, axis, [(0, 1), (1, 0)])
    return (keep.astype(jnp.float32) + got.astype(jnp.float32)).astype(jnp.bfloat16)


def make_per_device(expert_axes, mp_axes, experts, mp_count, n_chunks=2):
    def per_device(hidden_in, norm_gain, router_w, choices, w_gate, w_up, w_down):
        tokens_dev, model_width = hidden_in.shape
        capacity = 3 * tokens_dev // experts
        slice_width = model_width // mp_count
        rows_total = experts * capacity
        wide_in = hidden_in.astype(jnp.float32)
        normed = (
            wide_in
            * lax.rsqrt(jnp.mean(wide_in * wide_in, axis=1, keepdims=True) + eps_norm)
            * norm_gain
        ).astype(jnp.bfloat16)
        slot0, slot1, oh0, oh1 = pair_slots(choices, experts)
        chunk = capacity // n_chunks
        e0, e1 = choices[:, 0], choices[:, 1]
        chunk_rows = jnp.arange(experts * chunk, dtype=jnp.int32)
        column = lax.axis_index(mp_axes) * slice_width
        residual = lax.dynamic_slice_in_dim(hidden_in, column, slice_width, 1).astype(jnp.float32)
        mixture = None
        ff_share = w_gate.shape[2]
        gate_up = jnp.concatenate([w_gate[0], w_up[0]], axis=1)
        results = []
        for c in range(n_chunks):
            r0 = jnp.where(slot0 // chunk == c, (slot0 % chunk) * experts + e0, -1)
            r1 = jnp.where(slot1 // chunk == c, (slot1 % chunk) * experts + e1, -1)
            dispatch = (
                (r0[None, :] == chunk_rows[:, None]) | (r1[None, :] == chunk_rows[:, None])
            ).astype(jnp.bfloat16)
            part = jnp.dot(dispatch, normed, preferred_element_type=jnp.float32).astype(jnp.bfloat16)
            part = part.reshape(chunk, experts, model_width)
            arrived = lax.all_to_all(part, expert_axes, split_axis=1, concat_axis=1, tiled=True)
            expert_rows = arrived.reshape(chunk * experts, model_width)
            both = jnp.dot(expert_rows, gate_up, preferred_element_type=jnp.float32)
            gate_proj, up_proj = both[:, :ff_share], both[:, ff_share:]
            hidden = (jax.nn.silu(gate_proj) * up_proj).astype(jnp.bfloat16)
            partial_t = lax.dot_general(
                w_down[0], hidden, (((0,), (1,)), ((), ())), preferred_element_type=jnp.float32
            ).astype(jnp.bfloat16)
            summed = lax.psum_scatter(partial_t, mp_axes[0], scatter_dimension=0, tiled=True)
            halves = lax.axis_size(mp_axes[1])
            blocks = summed.reshape(halves, slice_width, chunk, experts).transpose(2, 3, 0, 1)
            blocks = blocks.reshape(chunk, experts * halves, slice_width)
            got = lax.all_to_all(blocks, expert_axes + mp_axes[1:], split_axis=1, concat_axis=1, tiled=True)
            got = got.reshape(chunk, experts, halves, slice_width).astype(jnp.float32).sum(axis=2)
            returned = got.astype(jnp.bfloat16).reshape(chunk * experts, slice_width)
            results.append((r0, r1, returned))
        logits = jnp.dot(normed, router_w, preferred_element_type=jnp.float32)
        w0, w1 = pair_weights(logits, oh0, oh1)
        dims = (((1,), (0,)), ((), ()))
        for r0, r1, returned in results:
            sel0 = (r0[:, None] == chunk_rows[None, :]).astype(jnp.bfloat16)
            sel1 = (r1[:, None] == chunk_rows[None, :]).astype(jnp.bfloat16)
            out0 = lax.dot_general(sel0, returned, dims, preferred_element_type=jnp.float32)
            out1 = lax.dot_general(sel1, returned, dims, preferred_element_type=jnp.float32)
            term = out0 * w0[:, None] + out1 * w1[:, None]
            mixture = term if mixture is None else mixture + term
        return (residual + mixture).astype(jnp.bfloat16)

    return per_device


def x_parts(devices):
    coords = [getattr(d, "coords", None) for d in devices]
    if any(c is None for c in coords):
        return 1
    return len({c[0] for c in coords})


def solution(mesh):
    n_dp, n_expert, n_mp = (mesh.shape[a] for a in ("dp", "expert", "mp"))
    devs = np.asarray(mesh.devices).reshape(n_dp, n_expert, n_mp)
    ex = x_parts(devs[0, :, 0])
    mx = x_parts(devs[0, 0, :])
    if n_expert % ex or n_mp % mx:
        ex, mx = 1, 1
    fine = Mesh(
        devs.reshape(n_dp, n_expert // ex, ex, n_mp // mx, mx), ("dp", "ey", "ex", "mz", "mx")
    )
    expert_axes = ("ey", "ex")
    mp_axes = ("mz", "mx")
    tok = ("dp",) + expert_axes
    placed = (
        P(tok, None),
        P(),
        P(),
        P(tok, None),
        P(expert_axes, None, mp_axes),
        P(expert_axes, None, mp_axes),
        P(expert_axes, mp_axes, None),
    )
    return jax.shard_map(
        make_per_device(expert_axes, mp_axes, n_expert, n_mp),
        mesh=fine,
        in_specs=placed,
        out_specs=P(tok, mp_axes),
        check_vma=False,
    )
```

```python
import numpy as np

import jax
import jax.numpy as jnp
from jax import lax
from jax.sharding import Mesh
from jax.sharding import PartitionSpec as P

eps_norm = 1e-06


def pair_slots(choices, experts):
    tokens = choices.shape[0]
    ids = jnp.arange(experts, dtype=jnp.int32)[None, :]
    oh0 = (choices[:, 0:1] == ids).astype(jnp.float32)
    oh1 = (choices[:, 1:2] == ids).astype(jnp.float32)
    tri = (
        jnp.arange(tokens, dtype=jnp.int32)[None, :] < jnp.arange(tokens, dtype=jnp.int32)[:, None]
    ).astype(jnp.bfloat16)
    cnt = jnp.dot(tri, (oh0 + oh1).astype(jnp.bfloat16), preferred_element_type=jnp.float32)
    slot0 = jnp.sum(cnt * oh0, axis=1)
    slot1 = jnp.sum((cnt + oh0) * oh1, axis=1)
    return slot0.astype(jnp.int32), slot1.astype(jnp.int32), oh0, oh1


def pair_weights(logits, oh0, oh1):
    picked0 = jnp.sum(logits * oh0, axis=1)
    picked1 = jnp.sum(logits * oh1, axis=1)
    first_weight = jax.nn.sigmoid(picked0 - picked1)
    return first_weight, 1.0 - first_weight


def pair_exchange(summed, axis):
    n = lax.axis_size(axis)
    if n == 1:
        return summed
    own = lax.axis_index(axis)
    width = summed.shape[0] // 2
    keep = lax.dynamic_slice_in_dim(summed, own * width, width, 0)
    give = lax.dynamic_slice_in_dim(summed, (1 - own) * width, width, 0)
    got = lax.ppermute(give, axis, [(0, 1), (1, 0)])
    return (keep.astype(jnp.float32) + got.astype(jnp.float32)).astype(jnp.bfloat16)


def make_per_device(expert_axes, mp_axes, experts, mp_count, n_chunks=2, tc_rows=320):
    def per_device(hidden_in, norm_gain, router_w, choices, w_gate, w_up, w_down):
        tokens_dev, model_width = hidden_in.shape
        capacity = 3 * tokens_dev // experts
        slice_width = model_width // mp_count
        rows_total = experts * capacity
        wide_in = hidden_in.astype(jnp.float32)
        normed = (
            wide_in
            * lax.rsqrt(jnp.mean(wide_in * wide_in, axis=1, keepdims=True) + eps_norm)
            * norm_gain
        ).astype(jnp.bfloat16)
        slot0, slot1, oh0, oh1 = pair_slots(choices, experts)
        chunk = capacity // n_chunks
        e0, e1 = choices[:, 0], choices[:, 1]
        chunk_rows = jnp.arange(experts * chunk, dtype=jnp.int32)
        column = lax.axis_index(mp_axes) * slice_width
        residual = lax.dynamic_slice_in_dim(hidden_in, column, slice_width, 1).astype(jnp.float32)
        mixture = None
        ff_share = w_gate.shape[2]
        gate_up = jnp.concatenate([w_gate[0], w_up[0]], axis=1)
        results = []
        for c in range(n_chunks):
            r0 = jnp.where(slot0 // chunk == c, e0 * chunk + slot0 % chunk, -1)
            r1 = jnp.where(slot1 // chunk == c, e1 * chunk + slot1 % chunk, -1)
            dispatch = (
                (r0[None, :] == chunk_rows[:, None]) | (r1[None, :] == chunk_rows[:, None])
            ).astype(jnp.bfloat16)
            part = jnp.dot(dispatch, normed, preferred_element_type=jnp.float32).astype(jnp.bfloat16)
            part = part.reshape(experts, chunk, model_width)
            if results:
                part = lax.optimization_barrier((part, previous))[0]
            arrived = lax.all_to_all(part, expert_axes, split_axis=0, concat_axis=0, tiled=True)
            expert_rows = arrived.reshape(experts * chunk, model_width)
            both = jnp.dot(expert_rows, gate_up, preferred_element_type=jnp.float32)
            gate_proj, up_proj = both[:, :ff_share], both[:, ff_share:]
            hidden = (jax.nn.silu(gate_proj) * up_proj).astype(jnp.bfloat16)
            partial_t = lax.dot_general(
                w_down[0], hidden, (((0,), (1,)), ((), ())), preferred_element_type=jnp.float32
            ).astype(jnp.bfloat16)
            previous = partial_t
            if c == n_chunks - 1 and tc_rows:
                sc_rows = experts * chunk - tc_rows
                on_sc = lax.psum_scatter(partial_t[:, :sc_rows], mp_axes[0], scatter_dimension=0, tiled=True)
                z_parts = lax.axis_size(mp_axes[0])
                on_tc = partial_t[:, sc_rows:].reshape(z_parts, model_width // z_parts, tc_rows)
                on_tc = lax.all_to_all(on_tc, mp_axes[0], split_axis=0, concat_axis=0, tiled=True)
                on_tc = on_tc.astype(jnp.float32).sum(axis=0).astype(jnp.bfloat16)
                summed = jnp.concatenate([on_sc, on_tc], axis=1)
            else:
                summed = lax.psum_scatter(partial_t, mp_axes[0], scatter_dimension=0, tiled=True)
            halves = lax.axis_size(mp_axes[1])
            blocks = summed.reshape(halves, slice_width, experts, chunk).transpose(2, 0, 1, 3)
            blocks = blocks.reshape(experts * halves, slice_width, chunk)
            got = lax.all_to_all(blocks, expert_axes + mp_axes[1:], split_axis=0, concat_axis=0, tiled=True)
            got = got.reshape(experts, halves, slice_width, chunk).astype(jnp.float32).sum(axis=1)
            returned = got.astype(jnp.bfloat16).transpose(1, 0, 2).reshape(slice_width, experts * chunk)
            results.append((r0, r1, returned))
        logits = jnp.dot(normed, router_w, preferred_element_type=jnp.float32)
        w0, w1 = pair_weights(logits, oh0, oh1)
        dims = (((1,), (1,)), ((), ()))
        for r0, r1, returned in results:
            sel0 = (r0[:, None] == chunk_rows[None, :]).astype(jnp.bfloat16)
            sel1 = (r1[:, None] == chunk_rows[None, :]).astype(jnp.bfloat16)
            out0 = lax.dot_general(sel0, returned, dims, preferred_element_type=jnp.float32)
            out1 = lax.dot_general(sel1, returned, dims, preferred_element_type=jnp.float32)
            term = out0 * w0[:, None] + out1 * w1[:, None]
            mixture = term if mixture is None else mixture + term
        return (residual + mixture).astype(jnp.bfloat16)

    return per_device


def x_parts(devices):
    coords = [getattr(d, "coords", None) for d in devices]
    if any(c is None for c in coords):
        return 1
    return len({c[0] for c in coords})


def solution(mesh):
    n_dp, n_expert, n_mp = (mesh.shape[a] for a in ("dp", "expert", "mp"))
    devs = np.asarray(mesh.devices).reshape(n_dp, n_expert, n_mp)
    ex = x_parts(devs[0, :, 0])
    mx = x_parts(devs[0, 0, :])
    if n_expert % ex or n_mp % mx:
        ex, mx = 1, 1
    fine = Mesh(
        devs.reshape(n_dp, n_expert // ex, ex, n_mp // mx, mx), ("dp", "ey", "ex", "mz", "mx")
    )
    expert_axes = ("ey", "ex")
    mp_axes = ("mz", "mx")
    tok = ("dp",) + expert_axes
    placed = (
        P(tok, None),
        P(),
        P(),
        P(tok, None),
        P(expert_axes, None, mp_axes),
        P(expert_axes, None, mp_axes),
        P(expert_axes, mp_axes, None),
    )
    return jax.shard_map(
        make_per_device(expert_axes, mp_axes, n_expert, n_mp),
        mesh=fine,
        in_specs=placed,
        out_specs=P(tok, mp_axes),
        check_vma=False,
    )
```

```python
import numpy as np

import jax
import jax.numpy as jnp
from jax import lax
from jax.sharding import Mesh
from jax.sharding import PartitionSpec as P

eps_norm = 1e-06


def pair_slots(choices, experts):
    tokens = choices.shape[0]
    ids = jnp.arange(experts, dtype=jnp.int32)[None, :]
    oh0 = (choices[:, 0:1] == ids).astype(jnp.float32)
    oh1 = (choices[:, 1:2] == ids).astype(jnp.float32)
    tri = (
        jnp.arange(tokens, dtype=jnp.int32)[None, :] < jnp.arange(tokens, dtype=jnp.int32)[:, None]
    ).astype(jnp.bfloat16)
    cnt = jnp.dot(tri, (oh0 + oh1).astype(jnp.bfloat16), preferred_element_type=jnp.float32)
    slot0 = jnp.sum(cnt * oh0, axis=1)
    slot1 = jnp.sum((cnt + oh0) * oh1, axis=1)
    return slot0.astype(jnp.int32), slot1.astype(jnp.int32), oh0, oh1


def pair_weights(logits, oh0, oh1):
    picked0 = jnp.sum(logits * oh0, axis=1)
    picked1 = jnp.sum(logits * oh1, axis=1)
    first_weight = jax.nn.sigmoid(picked0 - picked1)
    return first_weight, 1.0 - first_weight


def pair_exchange(summed, axis):
    n = lax.axis_size(axis)
    if n == 1:
        return summed
    own = lax.axis_index(axis)
    width = summed.shape[0] // 2
    keep = lax.dynamic_slice_in_dim(summed, own * width, width, 0)
    give = lax.dynamic_slice_in_dim(summed, (1 - own) * width, width, 0)
    got = lax.ppermute(give, axis, [(0, 1), (1, 0)])
    return (keep.astype(jnp.float32) + got.astype(jnp.float32)).astype(jnp.bfloat16)


def make_per_device(expert_axes, mp_axes, experts, mp_count, n_chunks=2):
    def per_device(hidden_in, norm_gain, router_w, choices, w_gate, w_up, w_down):
        tokens_dev, model_width = hidden_in.shape
        capacity = 3 * tokens_dev // experts
        slice_width = model_width // mp_count
        rows_total = experts * capacity
        wide_in = hidden_in.astype(jnp.float32)
        normed = (
            wide_in
            * lax.rsqrt(jnp.mean(wide_in * wide_in, axis=1, keepdims=True) + eps_norm)
            * norm_gain
        ).astype(jnp.bfloat16)
        slot0, slot1, oh0, oh1 = pair_slots(choices, experts)
        chunk = capacity // n_chunks
        e0, e1 = choices[:, 0], choices[:, 1]
        chunk_rows = jnp.arange(experts * chunk, dtype=jnp.int32)
        column = lax.axis_index(mp_axes) * slice_width
        residual = lax.dynamic_slice_in_dim(hidden_in, column, slice_width, 1).astype(jnp.float32)
        mixture = None
        ff_share = w_gate.shape[2]
        gate_up = jnp.concatenate([w_gate[0], w_up[0]], axis=1)
        results = []
        for c in range(n_chunks):
            r0 = jnp.where(slot0 // chunk == c, e0 * chunk + slot0 % chunk, -1)
            r1 = jnp.where(slot1 // chunk == c, e1 * chunk + slot1 % chunk, -1)
            dispatch = (
                (r0[None, :] == chunk_rows[:, None]) | (r1[None, :] == chunk_rows[:, None])
            ).astype(jnp.bfloat16)
            part = jnp.dot(dispatch, normed, preferred_element_type=jnp.float32).astype(jnp.bfloat16)
            part = part.reshape(experts, chunk, model_width)
            arrived = lax.all_to_all(part, expert_axes, split_axis=0, concat_axis=0, tiled=True)
            expert_rows = arrived.reshape(experts * chunk, model_width)
            both = jnp.dot(expert_rows, gate_up, preferred_element_type=jnp.float32)
            gate_proj, up_proj = both[:, :ff_share], both[:, ff_share:]
            hidden = (jax.nn.silu(gate_proj) * up_proj).astype(jnp.bfloat16)
            partial_t = lax.dot_general(
                w_down[0], hidden, (((0,), (1,)), ((), ())), preferred_element_type=jnp.float32
            ).astype(jnp.bfloat16)
            summed = lax.psum_scatter(partial_t, mp_axes[0], scatter_dimension=0, tiled=True)
            halves = lax.axis_size(mp_axes[1])
            blocks = summed.reshape(halves, slice_width, experts, chunk).transpose(2, 0, 1, 3)
            blocks = blocks.reshape(experts * halves, slice_width, chunk)
            got = lax.all_to_all(blocks, expert_axes + mp_axes[1:], split_axis=0, concat_axis=0, tiled=True)
            got = got.reshape(experts, halves, slice_width, chunk).astype(jnp.float32).sum(axis=1)
            returned = got.astype(jnp.bfloat16).transpose(1, 0, 2).reshape(slice_width, experts * chunk)
            results.append((r0, r1, returned))
        logits = jnp.dot(normed, router_w, preferred_element_type=jnp.float32)
        w0, w1 = pair_weights(logits, oh0, oh1)
        dims = (((1,), (1,)), ((), ()))
        for r0, r1, returned in results:
            both_rows = jnp.concatenate([r0, r1])
            sel = (both_rows[:, None] == chunk_rows[None, :]).astype(jnp.bfloat16)
            out = lax.dot_general(sel, returned, dims, preferred_element_type=jnp.float32)
            term = out[:tokens_dev] * w0[:, None] + out[tokens_dev:] * w1[:, None]
            mixture = term if mixture is None else mixture + term
        return (residual + mixture).astype(jnp.bfloat16)

    return per_device


def x_parts(devices):
    coords = [getattr(d, "coords", None) for d in devices]
    if any(c is None for c in coords):
        return 1
    return len({c[0] for c in coords})


def solution(mesh):
    n_dp, n_expert, n_mp = (mesh.shape[a] for a in ("dp", "expert", "mp"))
    devs = np.asarray(mesh.devices).reshape(n_dp, n_expert, n_mp)
    ex = x_parts(devs[0, :, 0])
    mx = x_parts(devs[0, 0, :])
    if n_expert % ex or n_mp % mx:
        ex, mx = 1, 1
    fine = Mesh(
        devs.reshape(n_dp, n_expert // ex, ex, n_mp // mx, mx), ("dp", "ey", "ex", "mz", "mx")
    )
    expert_axes = ("ey", "ex")
    mp_axes = ("mz", "mx")
    tok = ("dp",) + expert_axes
    placed = (
        P(tok, None),
        P(),
        P(),
        P(tok, None),
        P(expert_axes, None, mp_axes),
        P(expert_axes, None, mp_axes),
        P(expert_axes, mp_axes, None),
    )
    return jax.shard_map(
        make_per_device(expert_axes, mp_axes, n_expert, n_mp),
        mesh=fine,
        in_specs=placed,
        out_specs=P(tok, mp_axes),
        check_vma=False,
    )
```

```python
import numpy as np

import jax
import jax.numpy as jnp
from jax import lax
from jax.sharding import Mesh
from jax.sharding import PartitionSpec as P

eps_norm = 1e-06


def pair_slots(choices, experts):
    tokens = choices.shape[0]
    ids = jnp.arange(experts, dtype=jnp.int32)[None, :]
    oh0 = (choices[:, 0:1] == ids).astype(jnp.float32)
    oh1 = (choices[:, 1:2] == ids).astype(jnp.float32)
    tri = (
        jnp.arange(tokens, dtype=jnp.int32)[None, :] < jnp.arange(tokens, dtype=jnp.int32)[:, None]
    ).astype(jnp.bfloat16)
    cnt = jnp.dot(tri, (oh0 + oh1).astype(jnp.bfloat16), preferred_element_type=jnp.float32)
    slot0 = jnp.sum(cnt * oh0, axis=1)
    slot1 = jnp.sum((cnt + oh0) * oh1, axis=1)
    return slot0.astype(jnp.int32), slot1.astype(jnp.int32), oh0, oh1


def pair_weights(logits, oh0, oh1):
    picked0 = jnp.sum(logits * oh0, axis=1)
    picked1 = jnp.sum(logits * oh1, axis=1)
    first_weight = jax.nn.sigmoid(picked0 - picked1)
    return first_weight, 1.0 - first_weight


def pair_exchange(summed, axis):
    n = lax.axis_size(axis)
    if n == 1:
        return summed
    own = lax.axis_index(axis)
    width = summed.shape[0] // 2
    keep = lax.dynamic_slice_in_dim(summed, own * width, width, 0)
    give = lax.dynamic_slice_in_dim(summed, (1 - own) * width, width, 0)
    got = lax.ppermute(give, axis, [(0, 1), (1, 0)])
    return (keep.astype(jnp.float32) + got.astype(jnp.float32)).astype(jnp.bfloat16)


def make_per_device(expert_axes, mp_axes, experts, mp_count):
    def per_device(hidden_in, norm_gain, router_w, choices, w_gate, w_up, w_down):
        tokens_dev, model_width = hidden_in.shape
        capacity = 3 * tokens_dev // experts
        slice_width = model_width // mp_count
        rows_total = experts * capacity
        wide_in = hidden_in.astype(jnp.float32)
        normed = (
            wide_in
            * lax.rsqrt(jnp.mean(wide_in * wide_in, axis=1, keepdims=True) + eps_norm)
            * norm_gain
        ).astype(jnp.bfloat16)
        slot0, slot1, oh0, oh1 = pair_slots(choices, experts)
        lead = capacity // 2 + capacity // 24
        sizes = [lead, capacity - lead]
        offsets = [0, lead]
        e0, e1 = choices[:, 0], choices[:, 1]
        column = lax.axis_index(mp_axes) * slice_width
        residual = lax.dynamic_slice_in_dim(hidden_in, column, slice_width, 1).astype(jnp.float32)
        mixture = None
        ff_share = w_gate.shape[2]
        gate_up = jnp.concatenate([w_gate[0], w_up[0]], axis=1)
        results = []
        for chunk, first in zip(sizes, offsets):
            chunk_rows = jnp.arange(experts * chunk, dtype=jnp.int32)
            inside0 = (slot0 >= first) & (slot0 < first + chunk)
            inside1 = (slot1 >= first) & (slot1 < first + chunk)
            r0 = jnp.where(inside0, e0 * chunk + slot0 - first, -1)
            r1 = jnp.where(inside1, e1 * chunk + slot1 - first, -1)
            dispatch = (
                (r0[None, :] == chunk_rows[:, None]) | (r1[None, :] == chunk_rows[:, None])
            ).astype(jnp.bfloat16)
            part = jnp.dot(dispatch, normed, preferred_element_type=jnp.float32).astype(jnp.bfloat16)
            part = part.reshape(experts, chunk, model_width)
            if results:
                part = lax.optimization_barrier((part, previous))[0]
            arrived = lax.all_to_all(part, expert_axes, split_axis=0, concat_axis=0, tiled=True)
            expert_rows = arrived.reshape(experts * chunk, model_width)
            both = jnp.dot(expert_rows, gate_up, preferred_element_type=jnp.float32)
            gate_proj, up_proj = both[:, :ff_share], both[:, ff_share:]
            hidden = (jax.nn.silu(gate_proj) * up_proj).astype(jnp.bfloat16)
            partial_t = lax.dot_general(
                w_down[0], hidden, (((0,), (1,)), ((), ())), preferred_element_type=jnp.float32
            ).astype(jnp.bfloat16)
            previous = partial_t
            summed = lax.psum_scatter(partial_t, mp_axes[0], scatter_dimension=0, tiled=True)
            halves = lax.axis_size(mp_axes[1])
            blocks = summed.reshape(halves, slice_width, experts, chunk).transpose(2, 0, 1, 3)
            blocks = blocks.reshape(experts * halves, slice_width, chunk)
            got = lax.all_to_all(blocks, expert_axes + mp_axes[1:], split_axis=0, concat_axis=0, tiled=True)
            got = got.reshape(experts, halves, slice_width, chunk).astype(jnp.float32).sum(axis=1)
            returned = got.astype(jnp.bfloat16).transpose(1, 0, 2).reshape(slice_width, experts * chunk)
            results.append((r0, r1, returned, chunk_rows))
        logits = jnp.dot(normed, router_w, preferred_element_type=jnp.float32)
        w0, w1 = pair_weights(logits, oh0, oh1)
        dims = (((1,), (1,)), ((), ()))
        for r0, r1, returned, chunk_rows in results:
            both_rows = jnp.concatenate([r0, r1])
            sel = (both_rows[:, None] == chunk_rows[None, :]).astype(jnp.bfloat16)
            out = lax.dot_general(sel, returned, dims, preferred_element_type=jnp.float32)
            term = out[:tokens_dev] * w0[:, None] + out[tokens_dev:] * w1[:, None]
            mixture = term if mixture is None else mixture + term
        return (residual + mixture).astype(jnp.bfloat16)

    return per_device


def x_parts(devices):
    coords = [getattr(d, "coords", None) for d in devices]
    if any(c is None for c in coords):
        return 1
    return len({c[0] for c in coords})


def solution(mesh):
    n_dp, n_expert, n_mp = (mesh.shape[a] for a in ("dp", "expert", "mp"))
    devs = np.asarray(mesh.devices).reshape(n_dp, n_expert, n_mp)
    ex = x_parts(devs[0, :, 0])
    mx = x_parts(devs[0, 0, :])
    if n_expert % ex or n_mp % mx:
        ex, mx = 1, 1
    fine = Mesh(
        devs.reshape(n_dp, n_expert // ex, ex, n_mp // mx, mx), ("dp", "ey", "ex", "mz", "mx")
    )
    expert_axes = ("ey", "ex")
    mp_axes = ("mz", "mx")
    tok = ("dp",) + expert_axes
    placed = (
        P(tok, None),
        P(),
        P(),
        P(tok, None),
        P(expert_axes, None, mp_axes),
        P(expert_axes, None, mp_axes),
        P(expert_axes, mp_axes, None),
    )
    return jax.shard_map(
        make_per_device(expert_axes, mp_axes, n_expert, n_mp),
        mesh=fine,
        in_specs=placed,
        out_specs=P(tok, mp_axes),
        check_vma=False,
    )
```

```python
import numpy as np

import jax
import jax.numpy as jnp
from jax import lax
from jax.sharding import Mesh
from jax.sharding import PartitionSpec as P

eps_norm = 1e-06


def pair_slots(choices, experts):
    tokens = choices.shape[0]
    ids = jnp.arange(experts, dtype=jnp.int32)[None, :]
    oh0 = (choices[:, 0:1] == ids).astype(jnp.float32)
    oh1 = (choices[:, 1:2] == ids).astype(jnp.float32)
    tri = (
        jnp.arange(tokens, dtype=jnp.int32)[None, :] < jnp.arange(tokens, dtype=jnp.int32)[:, None]
    ).astype(jnp.bfloat16)
    cnt = jnp.dot(tri, (oh0 + oh1).astype(jnp.bfloat16), preferred_element_type=jnp.float32)
    slot0 = jnp.sum(cnt * oh0, axis=1)
    slot1 = jnp.sum((cnt + oh0) * oh1, axis=1)
    return slot0.astype(jnp.int32), slot1.astype(jnp.int32), oh0, oh1


def pair_weights(logits, oh0, oh1):
    picked0 = jnp.sum(logits * oh0, axis=1)
    picked1 = jnp.sum(logits * oh1, axis=1)
    first_weight = jax.nn.sigmoid(picked0 - picked1)
    return first_weight, 1.0 - first_weight


def pair_exchange(summed, axis):
    n = lax.axis_size(axis)
    if n == 1:
        return summed
    own = lax.axis_index(axis)
    width = summed.shape[0] // 2
    keep = lax.dynamic_slice_in_dim(summed, own * width, width, 0)
    give = lax.dynamic_slice_in_dim(summed, (1 - own) * width, width, 0)
    got = lax.ppermute(give, axis, [(0, 1), (1, 0)])
    return (keep.astype(jnp.float32) + got.astype(jnp.float32)).astype(jnp.bfloat16)


def make_per_device(expert_axes, mp_axes, experts, mp_count, n_chunks=2):
    def per_device(hidden_in, norm_gain, router_w, choices, w_gate, w_up, w_down):
        tokens_dev, model_width = hidden_in.shape
        capacity = 3 * tokens_dev // experts
        slice_width = model_width // mp_count
        rows_total = experts * capacity
        wide_in = hidden_in.astype(jnp.float32)
        squares = wide_in * wide_in
        high = squares.astype(jnp.bfloat16)
        low = (squares - high.astype(jnp.float32)).astype(jnp.bfloat16)
        ones = jnp.ones((model_width, 128), jnp.bfloat16)
        row_sums = jnp.dot(high, ones, preferred_element_type=jnp.float32) + jnp.dot(
            low, ones, preferred_element_type=jnp.float32
        )
        mean_sq = row_sums[:, :1] / model_width
        normed = (wide_in * lax.rsqrt(mean_sq + eps_norm) * norm_gain).astype(jnp.bfloat16)
        slot0, slot1, oh0, oh1 = pair_slots(choices, experts)
        chunk = capacity // n_chunks
        e0, e1 = choices[:, 0], choices[:, 1]
        chunk_rows = jnp.arange(experts * chunk, dtype=jnp.int32)
        column = lax.axis_index(mp_axes) * slice_width
        residual = lax.dynamic_slice_in_dim(hidden_in, column, slice_width, 1).astype(jnp.float32)
        mixture = None
        ff_share = w_gate.shape[2]
        gate_up = jnp.concatenate([w_gate[0], w_up[0]], axis=1)
        results = []
        for c in range(n_chunks):
            r0 = jnp.where(slot0 // chunk == c, e0 * chunk + slot0 % chunk, -1)
            r1 = jnp.where(slot1 // chunk == c, e1 * chunk + slot1 % chunk, -1)
            dispatch = (
                (r0[None, :] == chunk_rows[:, None]) | (r1[None, :] == chunk_rows[:, None])
            ).astype(jnp.bfloat16)
            part = jnp.dot(dispatch, normed, preferred_element_type=jnp.float32).astype(jnp.bfloat16)
            part = part.reshape(experts, chunk, model_width)
            arrived = lax.all_to_all(part, expert_axes, split_axis=0, concat_axis=0, tiled=True)
            expert_rows = arrived.reshape(experts * chunk, model_width)
            both = jnp.dot(expert_rows, gate_up, preferred_element_type=jnp.float32)
            gate_proj, up_proj = both[:, :ff_share], both[:, ff_share:]
            hidden = (jax.nn.silu(gate_proj) * up_proj).astype(jnp.bfloat16)
            partial_t = lax.dot_general(
                w_down[0], hidden, (((0,), (1,)), ((), ())), preferred_element_type=jnp.float32
            ).astype(jnp.bfloat16)
            summed = lax.psum_scatter(partial_t, mp_axes[0], scatter_dimension=0, tiled=True)
            halves = lax.axis_size(mp_axes[1])
            blocks = summed.reshape(halves, slice_width, experts, chunk).transpose(2, 0, 1, 3)
            blocks = blocks.reshape(experts * halves, slice_width, chunk)
            got = lax.all_to_all(blocks, expert_axes + mp_axes[1:], split_axis=0, concat_axis=0, tiled=True)
            got = got.reshape(experts, halves, slice_width, chunk).astype(jnp.float32).sum(axis=1)
            returned = got.astype(jnp.bfloat16).transpose(1, 0, 2).reshape(slice_width, experts * chunk)
            results.append((r0, r1, returned))
        logits = jnp.dot(normed, router_w, preferred_element_type=jnp.float32)
        w0, w1 = pair_weights(logits, oh0, oh1)
        dims = (((1,), (1,)), ((), ()))
        for r0, r1, returned in results:
            both_rows = jnp.concatenate([r0, r1])
            sel = (both_rows[:, None] == chunk_rows[None, :]).astype(jnp.bfloat16)
            out = lax.dot_general(sel, returned, dims, preferred_element_type=jnp.float32)
            term = out[:tokens_dev] * w0[:, None] + out[tokens_dev:] * w1[:, None]
            mixture = term if mixture is None else mixture + term
        return (residual + mixture).astype(jnp.bfloat16)

    return per_device


def x_parts(devices):
    coords = [getattr(d, "coords", None) for d in devices]
    if any(c is None for c in coords):
        return 1
    return len({c[0] for c in coords})


def solution(mesh):
    n_dp, n_expert, n_mp = (mesh.shape[a] for a in ("dp", "expert", "mp"))
    devs = np.asarray(mesh.devices).reshape(n_dp, n_expert, n_mp)
    ex = x_parts(devs[0, :, 0])
    mx = x_parts(devs[0, 0, :])
    if n_expert % ex or n_mp % mx:
        ex, mx = 1, 1
    fine = Mesh(
        devs.reshape(n_dp, n_expert // ex, ex, n_mp // mx, mx), ("dp", "ey", "ex", "mz", "mx")
    )
    expert_axes = ("ey", "ex")
    mp_axes = ("mz", "mx")
    tok = ("dp",) + expert_axes
    placed = (
        P(tok, None),
        P(),
        P(),
        P(tok, None),
        P(expert_axes, None, mp_axes),
        P(expert_axes, None, mp_axes),
        P(expert_axes, mp_axes, None),
    )
    return jax.shard_map(
        make_per_device(expert_axes, mp_axes, n_expert, n_mp),
        mesh=fine,
        in_specs=placed,
        out_specs=P(tok, mp_axes),
        check_vma=False,
    )
```

```python
import numpy as np

import jax
import jax.numpy as jnp
from jax import lax
from jax.sharding import Mesh
from jax.sharding import PartitionSpec as P

eps_norm = 1e-06


def pair_slots(choices, experts):
    tokens = choices.shape[0]
    ids = jnp.arange(experts, dtype=jnp.int32)[None, :]
    oh0 = (choices[:, 0:1] == ids).astype(jnp.float32)
    oh1 = (choices[:, 1:2] == ids).astype(jnp.float32)
    tri = (
        jnp.arange(tokens, dtype=jnp.int32)[None, :] < jnp.arange(tokens, dtype=jnp.int32)[:, None]
    ).astype(jnp.bfloat16)
    cnt = jnp.dot(tri, (oh0 + oh1).astype(jnp.bfloat16), preferred_element_type=jnp.float32)
    slot0 = jnp.sum(cnt * oh0, axis=1)
    slot1 = jnp.sum((cnt + oh0) * oh1, axis=1)
    return slot0.astype(jnp.int32), slot1.astype(jnp.int32), oh0, oh1


def pair_weights(logits, oh0, oh1):
    picked0 = jnp.sum(logits * oh0, axis=1)
    picked1 = jnp.sum(logits * oh1, axis=1)
    first_weight = jax.nn.sigmoid(picked0 - picked1)
    return first_weight, 1.0 - first_weight


def pair_exchange(summed, axis):
    n = lax.axis_size(axis)
    if n == 1:
        return summed
    own = lax.axis_index(axis)
    width = summed.shape[0] // 2
    keep = lax.dynamic_slice_in_dim(summed, own * width, width, 0)
    give = lax.dynamic_slice_in_dim(summed, (1 - own) * width, width, 0)
    got = lax.ppermute(give, axis, [(0, 1), (1, 0)])
    return (keep.astype(jnp.float32) + got.astype(jnp.float32)).astype(jnp.bfloat16)


def make_per_device(expert_axes, mp_axes, experts, mp_count, n_chunks=2):
    def per_device(hidden_in, norm_gain, router_w, choices, w_gate, w_up, w_down):
        tokens_dev, model_width = hidden_in.shape
        capacity = 3 * tokens_dev // experts
        slice_width = model_width // mp_count
        rows_total = experts * capacity
        wide_in = hidden_in.astype(jnp.float32)
        squares = wide_in * wide_in
        high = squares.astype(jnp.bfloat16)
        low = (squares - high.astype(jnp.float32)).astype(jnp.bfloat16)
        ones = jnp.ones((model_width, 128), jnp.bfloat16)
        row_sums = jnp.dot(high, ones, preferred_element_type=jnp.float32) + jnp.dot(
            low, ones, preferred_element_type=jnp.float32
        )
        mean_sq = row_sums[:, :1] / model_width
        normed = (wide_in * lax.rsqrt(mean_sq + eps_norm) * norm_gain).astype(jnp.bfloat16)
        slot0, slot1, oh0, oh1 = pair_slots(choices, experts)
        chunk = capacity // n_chunks
        e0, e1 = choices[:, 0], choices[:, 1]
        chunk_rows = jnp.arange(experts * chunk, dtype=jnp.int32)
        column = lax.axis_index(mp_axes) * slice_width
        residual = lax.dynamic_slice_in_dim(hidden_in, column, slice_width, 1).astype(jnp.float32)
        mixture = None
        ff_share = w_gate.shape[2]
        gate_up = jnp.concatenate([w_gate[0], w_up[0]], axis=1)
        results = []
        for c in range(n_chunks):
            r0 = jnp.where(slot0 // chunk == c, e0 * chunk + slot0 % chunk, -1)
            r1 = jnp.where(slot1 // chunk == c, e1 * chunk + slot1 % chunk, -1)
            dispatch = (
                (r0[None, :] == chunk_rows[:, None]) | (r1[None, :] == chunk_rows[:, None])
            ).astype(jnp.bfloat16)
            part = jnp.dot(dispatch, normed, preferred_element_type=jnp.float32).astype(jnp.bfloat16)
            part = part.reshape(experts, chunk, model_width)
            arrived = lax.all_to_all(part, expert_axes, split_axis=0, concat_axis=0, tiled=True)
            expert_rows = arrived.reshape(experts * chunk, model_width)
            both = jnp.dot(expert_rows, gate_up, preferred_element_type=jnp.float32)
            gate_proj, up_proj = both[:, :ff_share], both[:, ff_share:]
            hidden = lax.optimization_barrier((jax.nn.silu(gate_proj) * up_proj).astype(jnp.bfloat16))
            partial_t = lax.dot_general(
                w_down[0], hidden, (((0,), (1,)), ((), ())), preferred_element_type=jnp.float32
            ).astype(jnp.bfloat16)
            summed = lax.psum_scatter(partial_t, mp_axes[0], scatter_dimension=0, tiled=True)
            halves = lax.axis_size(mp_axes[1])
            blocks = summed.reshape(halves, slice_width, experts, chunk).transpose(2, 0, 1, 3)
            blocks = blocks.reshape(experts * halves, slice_width, chunk)
            got = lax.all_to_all(blocks, expert_axes + mp_axes[1:], split_axis=0, concat_axis=0, tiled=True)
            got = got.reshape(experts, halves, slice_width, chunk).astype(jnp.float32).sum(axis=1)
            returned = got.astype(jnp.bfloat16).transpose(1, 0, 2).reshape(slice_width, experts * chunk)
            results.append((r0, r1, returned))
        logits = jnp.dot(normed, router_w, preferred_element_type=jnp.float32)
        w0, w1 = pair_weights(logits, oh0, oh1)
        dims = (((1,), (1,)), ((), ()))
        for r0, r1, returned in results:
            both_rows = jnp.concatenate([r0, r1])
            sel = (both_rows[:, None] == chunk_rows[None, :]).astype(jnp.bfloat16)
            out = lax.dot_general(sel, returned, dims, preferred_element_type=jnp.float32)
            term = out[:tokens_dev] * w0[:, None] + out[tokens_dev:] * w1[:, None]
            mixture = term if mixture is None else mixture + term
        return (residual + mixture).astype(jnp.bfloat16)

    return per_device


def x_parts(devices):
    coords = [getattr(d, "coords", None) for d in devices]
    if any(c is None for c in coords):
        return 1
    return len({c[0] for c in coords})


def solution(mesh):
    n_dp, n_expert, n_mp = (mesh.shape[a] for a in ("dp", "expert", "mp"))
    devs = np.asarray(mesh.devices).reshape(n_dp, n_expert, n_mp)
    ex = x_parts(devs[0, :, 0])
    mx = x_parts(devs[0, 0, :])
    if n_expert % ex or n_mp % mx:
        ex, mx = 1, 1
    fine = Mesh(
        devs.reshape(n_dp, n_expert // ex, ex, n_mp // mx, mx), ("dp", "ey", "ex", "mz", "mx")
    )
    expert_axes = ("ey", "ex")
    mp_axes = ("mz", "mx")
    tok = ("dp",) + expert_axes
    placed = (
        P(tok, None),
        P(),
        P(),
        P(tok, None),
        P(expert_axes, None, mp_axes),
        P(expert_axes, None, mp_axes),
        P(expert_axes, mp_axes, None),
    )
    return jax.shard_map(
        make_per_device(expert_axes, mp_axes, n_expert, n_mp),
        mesh=fine,
        in_specs=placed,
        out_specs=P(tok, mp_axes),
        check_vma=False,
    )
```

```python
import numpy as np

import jax
import jax.numpy as jnp
from jax import lax
from jax.sharding import Mesh
from jax.sharding import PartitionSpec as P

eps_norm = 1e-06


def pair_slots(choices, experts):
    tokens = choices.shape[0]
    ids = jnp.arange(experts, dtype=jnp.int32)[None, :]
    oh0 = (choices[:, 0:1] == ids).astype(jnp.float32)
    oh1 = (choices[:, 1:2] == ids).astype(jnp.float32)
    tri = (
        jnp.arange(tokens, dtype=jnp.int32)[None, :] < jnp.arange(tokens, dtype=jnp.int32)[:, None]
    ).astype(jnp.bfloat16)
    cnt = jnp.dot(tri, (oh0 + oh1).astype(jnp.bfloat16), preferred_element_type=jnp.float32)
    slot0 = jnp.sum(cnt * oh0, axis=1)
    slot1 = jnp.sum((cnt + oh0) * oh1, axis=1)
    return slot0.astype(jnp.int32), slot1.astype(jnp.int32), oh0, oh1


def pair_weights(logits, oh0, oh1):
    picked0 = jnp.sum(logits * oh0, axis=1)
    picked1 = jnp.sum(logits * oh1, axis=1)
    first_weight = jax.nn.sigmoid(picked0 - picked1)
    return first_weight, 1.0 - first_weight


def rms_norm(wide_in, norm_gain):
    model_width = wide_in.shape[1]
    squares = wide_in * wide_in
    high = squares.astype(jnp.bfloat16)
    low = (squares - high.astype(jnp.float32)).astype(jnp.bfloat16)
    ones = jnp.ones((model_width, 128), jnp.bfloat16)
    row_sums = jnp.dot(high, ones, preferred_element_type=jnp.float32) + jnp.dot(
        low, ones, preferred_element_type=jnp.float32
    )
    mean_sq = row_sums[:, :1] / model_width
    return (wide_in * lax.rsqrt(mean_sq + eps_norm) * norm_gain).astype(jnp.bfloat16)


def pair_exchange(summed, axis):
    n = lax.axis_size(axis)
    if n == 1:
        return summed
    own = lax.axis_index(axis)
    width = summed.shape[0] // 2
    keep = lax.dynamic_slice_in_dim(summed, own * width, width, 0)
    give = lax.dynamic_slice_in_dim(summed, (1 - own) * width, width, 0)
    got = lax.ppermute(give, axis, [(0, 1), (1, 0)])
    return (keep.astype(jnp.float32) + got.astype(jnp.float32)).astype(jnp.bfloat16)


def make_per_device(expert_axes, mp_axes, experts, mp_count, n_chunks=2):
    def per_device(hidden_in, norm_gain, router_w, choices, w_gate, w_up, w_down):
        tokens_dev, model_width = hidden_in.shape
        capacity = 3 * tokens_dev // experts
        slice_width = model_width // mp_count
        rows_total = experts * capacity
        wide_in = hidden_in.astype(jnp.float32)
        normed = rms_norm(wide_in, norm_gain)
        slot0, slot1, oh0, oh1 = pair_slots(choices, experts)
        chunk = capacity // n_chunks
        e0, e1 = choices[:, 0], choices[:, 1]
        chunk_rows = jnp.arange(experts * chunk, dtype=jnp.int32)
        column = lax.axis_index(mp_axes) * slice_width
        residual = lax.dynamic_slice_in_dim(hidden_in, column, slice_width, 1).astype(jnp.float32)
        mixture = None
        ff_share = w_gate.shape[2]
        gate_up = jnp.concatenate([w_gate[0], w_up[0]], axis=1)
        results = []
        for c in range(n_chunks):
            r0 = jnp.where(slot0 // chunk == c, e0 * chunk + slot0 % chunk, -1)
            r1 = jnp.where(slot1 // chunk == c, e1 * chunk + slot1 % chunk, -1)
            dispatch = (
                (r0[None, :] == chunk_rows[:, None]) | (r1[None, :] == chunk_rows[:, None])
            ).astype(jnp.bfloat16)
            part = jnp.dot(dispatch, normed, preferred_element_type=jnp.float32).astype(jnp.bfloat16)
            part = part.reshape(experts, chunk, model_width)
            arrived = lax.all_to_all(part, expert_axes, split_axis=0, concat_axis=0, tiled=True)
            expert_rows = arrived.reshape(experts * chunk, model_width)
            both = jnp.dot(expert_rows, gate_up, preferred_element_type=jnp.float32)
            gate_proj, up_proj = both[:, :ff_share], both[:, ff_share:]
            hidden = (jax.nn.silu(gate_proj) * up_proj).astype(jnp.bfloat16)
            partial_t = lax.dot_general(
                w_down[0], hidden, (((0,), (1,)), ((), ())), preferred_element_type=jnp.float32
            ).astype(jnp.bfloat16)
            previous = partial_t
            summed = lax.psum_scatter(partial_t, mp_axes[0], scatter_dimension=0, tiled=True)
            halves = lax.axis_size(mp_axes[1])
            blocks = summed.reshape(halves, slice_width, experts, chunk).transpose(2, 0, 1, 3)
            blocks = blocks.reshape(experts * halves, slice_width, chunk)
            got = lax.all_to_all(blocks, expert_axes + mp_axes[1:], split_axis=0, concat_axis=0, tiled=True)
            got = got.reshape(experts, halves, slice_width, chunk).astype(jnp.float32).sum(axis=1)
            returned = got.astype(jnp.bfloat16).transpose(1, 0, 2).reshape(slice_width, experts * chunk)
            results.append((r0, r1, returned))
        late_in = lax.optimization_barrier((hidden_in, previous))[0]
        late_normed = rms_norm(late_in.astype(jnp.float32), norm_gain)
        logits = jnp.dot(late_normed, router_w, preferred_element_type=jnp.float32)
        w0, w1 = pair_weights(logits, oh0, oh1)
        dims = (((1,), (1,)), ((), ()))
        for r0, r1, returned in results:
            both_rows = jnp.concatenate([r0, r1])
            sel = (both_rows[:, None] == chunk_rows[None, :]).astype(jnp.bfloat16)
            out = lax.dot_general(sel, returned, dims, preferred_element_type=jnp.float32)
            term = out[:tokens_dev] * w0[:, None] + out[tokens_dev:] * w1[:, None]
            mixture = residual + term if mixture is None else mixture + term
        return mixture.astype(jnp.bfloat16)

    return per_device


def x_parts(devices):
    coords = [getattr(d, "coords", None) for d in devices]
    if any(c is None for c in coords):
        return 1
    return len({c[0] for c in coords})


def solution(mesh):
    n_dp, n_expert, n_mp = (mesh.shape[a] for a in ("dp", "expert", "mp"))
    devs = np.asarray(mesh.devices).reshape(n_dp, n_expert, n_mp)
    ex = x_parts(devs[0, :, 0])
    mx = x_parts(devs[0, 0, :])
    if n_expert % ex or n_mp % mx:
        ex, mx = 1, 1
    fine = Mesh(
        devs.reshape(n_dp, n_expert // ex, ex, n_mp // mx, mx), ("dp", "ey", "ex", "mz", "mx")
    )
    expert_axes = ("ey", "ex")
    mp_axes = ("mz", "mx")
    tok = ("dp",) + expert_axes
    placed = (
        P(tok, None),
        P(),
        P(),
        P(tok, None),
        P(expert_axes, None, mp_axes),
        P(expert_axes, None, mp_axes),
        P(expert_axes, mp_axes, None),
    )
    return jax.shard_map(
        make_per_device(expert_axes, mp_axes, n_expert, n_mp),
        mesh=fine,
        in_specs=placed,
        out_specs=P(tok, mp_axes),
        check_vma=False,
    )
```
